256 devices in a mesh: replica: 16 (over z_lo, x, core), shard: 16 (over z_hi, y).
Axes of the slice: x: 4, y: 4, z: 8 (z_hi: 4, z_lo: 2; z = z_hi * 2 + z_lo), core: 2. Of those that a mesh axis runs over, the one named last changes fastest.
Arguments:
- tokens: bfloat16 [32768, 8192], P(('replica', 'shard')), may hold values from -6 to 6
- query_vectors: bfloat16 [32768, 8192], P(('replica', 'shard')), may hold values from -4.5 to 4.5
- key_vectors: bfloat16 [32768, 1024], P(('replica', 'shard')), may hold values from -4.5 to 4.5
- segment_ids: int32 [256, 128], P(('replica', 'shard')), may hold values from 0 to 7, never falling along the last dimension, each value on 1 to 32 neighbouring positions
- base_weight: bfloat16 [8192, 1024], P('shard'), may hold values from -0.0625 to 0.0625
- delta_values: bfloat16 [64, 64, 64], replicated, may hold values from -0.1875 to 0.1875
- block_list: int32 [64, 2], replicated, may hold values from 0 to 127, as said below
- out_cotangent: bfloat16 [32768, 8192], P(('replica', 'shard')), may hold values from -6 to 6
Outputs:
- attention: bfloat16 [32768, 8192], P(('replica', 'shard'))
- input_grad: bfloat16 [32768, 8192], P(('replica', 'shard'))
- delta_grad: float32 [64, 64, 64], P('shard')
The draws below stay inside these ranges and needn't reach their ends.
Inputs may be any that keep to these rules, and one draw needn't show every extreme that they name: `segment_ids`: segment ids never fall along a row; each row is the tokens of one device. `block_list`: every row names a distinct pair (row block below 128, column block below 16).
All inputs are finite; a program needn't handle non-finite values.
Results may differ from the reference program's by a relative error of at most 0.0056.
Values may be sent and summed in bfloat16 or wider, within the bound.
No kernel may reach another device: no remote copies, remote signals or barrier semaphores. Data moves between devices by JAX's collectives and lax.ppermute only.
A program may use at most 128 MiB of HBM per device.

```python
import math
import jax
import jax.numpy as jnp
import numpy as np
from jax import lax

D = 8192
QH = 64
KVH = 8
HD = 128
BLK = 64
NB = 64
SEGS = 8
TOK_DEV = 128
GROUPS = 256
TOKENS = 32768


def draw_query_vectors(key, part):
    sample = jnp.clip(jax.random.normal(jax.random.fold_in(key, 1), (TOKENS, QH * HD), jnp.float32), -4.5, 4.5)
    return sample.astype(jnp.bfloat16)


def draw_key_vectors(key, part):
    sample = jnp.clip(jax.random.normal(jax.random.fold_in(key, 2), (TOKENS, KVH * HD), jnp.float32), -4.5, 4.5)
    return sample.astype(jnp.bfloat16)


def draw_block_list(key, part):
    col_blocks = KVH * HD // BLK
    total = D // BLK * col_blocks
    fixed_pair = (D // BLK - 1) * col_blocks
    others = jax.random.permutation(jax.random.fold_in(key, 3), total - 1)[:NB - 1].astype(jnp.int32)
    others = others + (others >= fixed_pair).astype(jnp.int32)
    picked = jnp.concatenate([jnp.full((1,), fixed_pair, jnp.int32), others])
    offset = jax.random.randint(jax.random.fold_in(key, 5), (), 0, NB)
    picked = jnp.roll(picked, offset)
    row_index = picked // col_blocks
    col_index = picked % col_blocks
    return jnp.stack([row_index, col_index], axis=1).astype(jnp.int32)


def block_levels(stream_key, extent, cuts, smallest, top_value):
    def one(dim, blocks):
        draws = jax.random.uniform(jax.random.fold_in(jax.random.fold_in(stream_key, 6), dim), (blocks,), jnp.float32, smallest / len(cuts), top_value / len(cuts))
        return jnp.repeat(jnp.exp(draws), extent[dim] // blocks).reshape((-1,) + (1,) * (len(extent) - dim - 1))

    gain = one(*cuts[0])
    for cut in cuts[1:]:
        gain = gain * one(*cut)
    return gain


def length_profile(count, total, most, slope):
    loads = [(1 << 20) // math.isqrt(grade ** slope) + 1 for grade in range(2, count + 1)]
    spare, holding = total - most - (count - 1), [1] * (count - 1)
    while spare > 0:
        movable = [i for i in range(count - 1) if holding[i] < most]
        mass, left = sum([loads[i] for i in movable]), spare
        for i in movable:
            extra = min(most - holding[i], max(1, left * loads[i] // mass), spare)
            holding[i] = holding[i] + extra
            spare = spare - extra
    return np.array([most] + holding)


def uneven_parts(key, amount, total, reach, lean):
    if amount == 2:
        one = jax.random.randint(key, (), max(1, total - reach), min(reach, total - 1) + 1)
        return jnp.stack([one, total - one])
    sizes = jnp.asarray(length_profile(amount, total, reach, lean), jnp.int32)
    twos = (amount - 1) // 2
    donor, sink = sizes[1:1 + 2 * twos:2], sizes[2:2 + 2 * twos:2]
    room = jnp.minimum(donor - 1, reach - sink)
    passed = jax.random.randint(jax.random.fold_in(key, 1), (twos,), 0, 1 << 20) % (room + 1)
    sizes = sizes.at[1:1 + 2 * twos:2].set(donor - passed).at[2:2 + 2 * twos:2].set(sink + passed)
    return sizes[jax.random.permutation(jax.random.fold_in(key, 2), amount)]


def noise(rng, dims, spread, reach, cuts=(), held_as=jnp.bfloat16):
    level = block_levels(rng, dims, cuts, -0.22, 0.18) if cuts else 1.0
    drawn = jax.random.normal(rng, dims, jnp.float32) * spread * level
    return jnp.minimum(jnp.maximum(drawn, -reach), reach).astype(held_as)


def setup_inputs(seed: int = 0) -> dict:
    streams_of = jax.random.split(jax.random.key(seed), 9)
    return {
        "tokens": noise(streams_of[0], (TOKENS, D), 1.0, 6.0, ((0, 256),)),
        "query_vectors": draw_query_vectors(jax.random.fold_in(streams_of[8], 71), 0),
        "key_vectors": draw_key_vectors(jax.random.fold_in(streams_of[8], 71), 0),
        "segment_ids": jax.vmap(lambda own: jnp.searchsorted(jnp.cumsum(uneven_parts(own, SEGS, TOK_DEV, TOK_DEV // 4, 1)), jnp.arange(TOK_DEV), side="right"))(jax.random.split(streams_of[3], GROUPS)).reshape((GROUPS, TOK_DEV)).astype(jnp.int32),
        "base_weight": noise(streams_of[4], (D, KVH * HD), D ** -0.5, 0.0625, ((0, 16),)),
        "delta_values": noise(streams_of[5], (NB, BLK, BLK), (16 * BLK) ** -0.5, 0.1875),
        "block_list": draw_block_list(jax.random.fold_in(streams_of[8], 71), 0),
        "out_cotangent": noise(streams_of[7], (TOKENS, QH * HD), 1.0, 6.0, ((0, 256),)),
    }


def reference(tokens, query_vectors, key_vectors, segment_ids, base_weight, delta_values, block_list, out_cotangent):
    row_index = block_list[:, 0].astype(jnp.int32)
    col_index = block_list[:, 1].astype(jnp.int32)
    delta_float = delta_values.astype(jnp.float32)
    groups = QH // KVH

    def one_group(running, pieces):
        tok_block, query_block, key_block, seg_row, cot_block = pieces
        tok_rows = tok_block.shape[0]
        picked = tok_block.reshape(tok_rows, D // BLK, BLK)[:, row_index].astype(jnp.float32)
        block_term = jnp.einsum('tbk,bkj->tbj', picked, delta_float)
        sparse_part = jnp.zeros((tok_rows, KVH * HD // BLK, BLK), jnp.float32).at[:, col_index].add(block_term)
        dense_part = jnp.dot(tok_block, base_weight, preferred_element_type=jnp.float32)
        values = (dense_part + sparse_part.reshape(tok_rows, KVH * HD)).astype(jnp.bfloat16)
        query_heads = query_block.reshape(tok_rows, KVH, groups, HD).astype(jnp.float32)
        key_heads = key_block.reshape(tok_rows, KVH, HD).astype(jnp.float32)
        scores = jnp.einsum('tgsd,ugd->gstu', query_heads, key_heads) * (1.0 / math.sqrt(HD))
        position = jnp.arange(tok_rows, dtype=jnp.int32)
        allowed = (position[None, :] <= position[:, None]) & (seg_row[:, None] == seg_row[None, :])
        scores = jnp.where(allowed, scores, -1e+30)
        row_max = lax.optimization_barrier(jnp.max(scores, axis=-1, keepdims=True))
        exp_scores = jnp.exp(scores - row_max)
        attn_probs = (exp_scores / lax.optimization_barrier(jnp.sum(exp_scores, axis=-1, keepdims=True))).astype(jnp.bfloat16)
        probs_float = attn_probs.astype(jnp.float32)
        value_heads = values.reshape(tok_rows, KVH, HD).astype(jnp.float32)
        attention = jnp.einsum('gstu,ugd->tgsd', probs_float, value_heads).reshape(tok_rows, QH * HD).astype(jnp.bfloat16)
        cotangent_heads = cot_block.reshape(tok_rows, KVH, groups, HD).astype(jnp.float32)
        value_grad = jnp.einsum('gstu,tgsd->ugd', probs_float, cotangent_heads).reshape(tok_rows, KVH * HD).astype(jnp.bfloat16)
        dense_back = lax.dot_general(value_grad, base_weight, (((1,), (1,)), ((), ())), preferred_element_type=jnp.float32)
        chosen = value_grad.reshape(tok_rows, KVH * HD // BLK, BLK)[:, col_index].astype(jnp.float32)
        back_term = jnp.einsum('tbj,bkj->tbk', chosen, delta_float)
        spread_back = jnp.zeros((tok_rows, D // BLK, BLK), jnp.float32).at[:, row_index].add(back_term)
        input_grad = (dense_back + spread_back.reshape(tok_rows, D)).astype(jnp.bfloat16)
        grad_term = jnp.einsum('tbk,tbj->bkj', picked, chosen)
        return (running + grad_term, (attention, input_grad))
    pieces = (tokens.reshape(GROUPS, TOK_DEV, D), query_vectors.reshape(GROUPS, TOK_DEV, QH * HD), key_vectors.reshape(GROUPS, TOK_DEV, KVH * HD), segment_ids, out_cotangent.reshape(GROUPS, TOK_DEV, QH * HD))
    start_sum = jnp.zeros((NB, BLK, BLK), jnp.float32)
    grad_total, outputs = lax.scan(one_group, start_sum, pieces)
    attention = outputs[0].reshape(TOKENS, QH * HD)
    input_grad = outputs[1].reshape(TOKENS, D)
    delta_grad = grad_total * (1.0 / math.sqrt(TOKENS))
    return (attention, input_grad, delta_grad)
```

```python
import math

import jax
import jax.numpy as jnp
from jax import lax
from jax.sharding import Mesh
from jax.sharding import PartitionSpec as P

D = 8192
QH = 64
KVH = 8
HD = 128
BLK = 64

REPLICA = ("zl", "x", "c")
SHARD = ("zh", "y")
ALL = REPLICA + SHARD
PIECE = ("x", "c")


def block_tables(block_list):
    row_hot = (block_list[:, 0:1] == jnp.arange(D // BLK, dtype=jnp.int32)[None, :]).astype(
        jnp.bfloat16
    )
    col_hot = (block_list[:, 1:2] == jnp.arange(KVH * HD // BLK, dtype=jnp.int32)[None, :]).astype(
        jnp.bfloat16
    )
    return (row_hot, col_hot)


def gather_weight(base_weight):
    rows = base_weight.shape[0]
    pieces = lax.axis_size("x") * lax.axis_size("c")
    width = rows // pieces
    me = lax.axis_index("x") * lax.axis_size("c") + lax.axis_index("c")
    piece = lax.dynamic_slice_in_dim(base_weight, me * width, width, 0)
    by_shard = lax.all_gather(piece, SHARD, axis=0, tiled=False)
    whole = lax.all_gather(by_shard, PIECE, axis=1, tiled=True)
    return whole.reshape(-1, base_weight.shape[1])


def reduce_delta(grad_term):
    n_shard = lax.axis_size(SHARD)
    n_rep = lax.axis_size(REPLICA)
    nb = grad_term.shape[0]
    flat = grad_term.reshape(n_shard, -1)
    mine = lax.all_to_all(flat, SHARD, 0, 0, tiled=False).sum(0)
    mine = mine.reshape(n_rep, -1)
    part = lax.all_to_all(mine, REPLICA, 0, 0, tiled=False).sum(0)
    spread = jnp.broadcast_to(part[None], (n_rep,) + part.shape)
    whole = lax.all_to_all(spread, REPLICA, 0, 0, tiled=False)
    return whole.reshape(nb // n_shard, BLK, BLK)


def local(
    tokens,
    query_vectors,
    key_vectors,
    segment_ids,
    base_weight,
    delta_values,
    block_list,
    out_cotangent,
):
    tok_rows = tokens.shape[0]
    groups = QH // KVH
    row_index = block_list[:, 0]
    col_index = block_list[:, 1]
    full_weight = gather_weight(base_weight)
    row_hot, col_hot = block_tables(block_list)
    picked = jnp.einsum(
        "trk,br->tbk",
        tokens.reshape(tok_rows, D // BLK, BLK),
        row_hot,
        preferred_element_type=jnp.float32,
    ).astype(jnp.bfloat16)
    query_heads = query_vectors.reshape(tok_rows, KVH, groups, HD)
    key_heads = key_vectors.reshape(tok_rows, KVH, HD)
    scores = jnp.einsum(
        "tgsd,ugd->gstu", query_heads, key_heads, preferred_element_type=jnp.float32
    ) * (1.0 / math.sqrt(HD))
    seg_row = segment_ids[0]
    position = jnp.arange(tok_rows, dtype=jnp.int32)
    allowed = (position[None, :] <= position[:, None]) & (seg_row[:, None] == seg_row[None, :])
    scores = jnp.where(allowed, scores, -1e30)
    row_max = jnp.max(scores, axis=-1, keepdims=True)
    exp_scores = jnp.exp(scores - row_max)
    attn_probs = (exp_scores / jnp.sum(exp_scores, axis=-1, keepdims=True)).astype(jnp.bfloat16)
    cotangent_heads = out_cotangent.reshape(tok_rows, KVH, groups, HD)
    value_grad = (
        jnp.einsum(
            "gstu,tgsd->ugd", attn_probs, cotangent_heads, preferred_element_type=jnp.float32
        )
        .reshape(tok_rows, KVH * HD)
        .astype(jnp.bfloat16)
    )
    chosen = jnp.einsum(
        "tcj,bc->tbj",
        value_grad.reshape(tok_rows, KVH * HD // BLK, BLK),
        col_hot,
        preferred_element_type=jnp.float32,
    ).astype(jnp.bfloat16)
    grad_scale = 1.0 / math.sqrt(tok_rows * lax.axis_size(ALL))
    grad_term = (
        jnp.einsum("tbk,tbj->bkj", picked, chosen, preferred_element_type=jnp.float32) * grad_scale
    )
    delta_grad = reduce_delta(grad_term)

    block_term = jnp.einsum(
        "tbk,bkj->tbj", picked, delta_values, preferred_element_type=jnp.float32
    )
    sparse_part = (
        jnp.zeros((tok_rows, KVH * HD // BLK, BLK), jnp.float32)
        .at[:, col_index]
        .add(block_term)
        .reshape(tok_rows, KVH * HD)
    )
    dense_part = jnp.dot(tokens, full_weight, preferred_element_type=jnp.float32)
    values = (dense_part + sparse_part).astype(jnp.bfloat16)
    value_heads = values.reshape(tok_rows, KVH, HD)
    attention = (
        jnp.einsum("gstu,ugd->tgsd", attn_probs, value_heads, preferred_element_type=jnp.float32)
        .reshape(tok_rows, QH * HD)
        .astype(jnp.bfloat16)
    )
    dense_back = lax.dot_general(
        value_grad, full_weight, (((1,), (1,)), ((), ())), preferred_element_type=jnp.float32
    )
    back_term = jnp.einsum("tbj,bkj->tbk", chosen, delta_values, preferred_element_type=jnp.float32)
    spread_back = (
        jnp.zeros((tok_rows, D // BLK, BLK), jnp.float32)
        .at[:, row_index]
        .add(back_term)
        .reshape(tok_rows, D)
    )
    input_grad = (dense_back + spread_back).astype(jnp.bfloat16)
    return (attention, input_grad, delta_grad)


def solution(mesh):
    n_shard = mesh.shape["shard"]
    n_rep = mesh.shape["replica"]
    fine = Mesh(
        mesh.devices.reshape(2, 4, n_rep // 8, 4, n_shard // 4), ALL
    )
    tok = P(ALL, None)
    return jax.shard_map(
        local,
        mesh=fine,
        in_specs=(tok, tok, tok, tok, P(SHARD, None), P(), P(), tok),
        out_specs=(tok, tok, P(SHARD, None, None)),
        check_vma=False,
    )
```

```python
import math

import jax
import jax.numpy as jnp
from jax import lax
from jax.sharding import Mesh
from jax.sharding import PartitionSpec as P

D = 8192
QH = 64
KVH = 8
HD = 128
BLK = 64

REPLICA = ("zl", "x", "c")
SHARD = ("zh", "y")
ALL = REPLICA + SHARD
PIECE = ("x", "c")


def block_tables(block_list):
    row_hot = (block_list[:, 0:1] == jnp.arange(D // BLK, dtype=jnp.int32)[None, :]).astype(
        jnp.bfloat16
    )
    col_hot = (block_list[:, 1:2] == jnp.arange(KVH * HD // BLK, dtype=jnp.int32)[None, :]).astype(
        jnp.bfloat16
    )
    return (row_hot, col_hot)


def gather_pieces(base_weight):
    rows = base_weight.shape[0]
    pieces = lax.axis_size("x") * lax.axis_size("c")
    width = rows // pieces
    me = lax.axis_index("x") * lax.axis_size("c") + lax.axis_index("c")
    piece = lax.dynamic_slice_in_dim(base_weight, me * width, width, 0)
    return lax.all_gather(piece, SHARD, axis=0, tiled=False)


def gather_rest(by_shard):
    whole = lax.all_gather(by_shard, PIECE, axis=1, tiled=True)
    return whole.reshape(-1, whole.shape[-1])


def reduce_delta(grad_term, by_shard):
    n_shard = lax.axis_size(SHARD)
    n_rep = lax.axis_size(REPLICA)
    nb = grad_term.shape[0]
    flat = grad_term.reshape(n_shard, -1)
    mine = lax.all_to_all(flat, SHARD, 0, 0, tiled=False).sum(0)
    mine, by_shard = lax.optimization_barrier((mine, by_shard))
    full_weight = gather_rest(by_shard)
    mine = mine.reshape(n_rep, -1)
    part = lax.all_to_all(mine, REPLICA, 0, 0, tiled=False).sum(0)
    spread = jnp.broadcast_to(part[None], (n_rep,) + part.shape)
    whole = lax.all_to_all(spread, REPLICA, 0, 0, tiled=False)
    return whole.reshape(nb // n_shard, BLK, BLK), full_weight


def local(
    tokens,
    query_vectors,
    key_vectors,
    segment_ids,
    base_weight,
    delta_values,
    block_list,
    out_cotangent,
):
    tok_rows = tokens.shape[0]
    groups = QH // KVH
    row_index = block_list[:, 0]
    col_index = block_list[:, 1]
    by_shard = gather_pieces(base_weight)
    row_hot, col_hot = block_tables(block_list)
    picked = jnp.einsum(
        "trk,br->tbk",
        tokens.reshape(tok_rows, D // BLK, BLK),
        row_hot,
        preferred_element_type=jnp.float32,
    ).astype(jnp.bfloat16)
    query_heads = query_vectors.reshape(tok_rows, KVH, groups, HD)
    key_heads = key_vectors.reshape(tok_rows, KVH, HD)
    scores = jnp.einsum(
        "tgsd,ugd->gstu", query_heads, key_heads, preferred_element_type=jnp.float32
    ) * (1.0 / math.sqrt(HD))
    seg_row = segment_ids[0]
    position = jnp.arange(tok_rows, dtype=jnp.int32)
    allowed = (position[None, :] <= position[:, None]) & (seg_row[:, None] == seg_row[None, :])
    scores = jnp.where(allowed, scores, -1e30)
    row_max = jnp.max(scores, axis=-1, keepdims=True)
    exp_scores = jnp.exp(scores - row_max)
    attn_probs = (exp_scores / jnp.sum(exp_scores, axis=-1, keepdims=True)).astype(jnp.bfloat16)
    cotangent_heads = out_cotangent.reshape(tok_rows, KVH, groups, HD)
    value_grad = (
        jnp.einsum(
            "gstu,tgsd->ugd", attn_probs, cotangent_heads, preferred_element_type=jnp.float32
        )
        .reshape(tok_rows, KVH * HD)
        .astype(jnp.bfloat16)
    )
    chosen = jnp.einsum(
        "tcj,bc->tbj",
        value_grad.reshape(tok_rows, KVH * HD // BLK, BLK),
        col_hot,
        preferred_element_type=jnp.float32,
    ).astype(jnp.bfloat16)
    grad_scale = 1.0 / math.sqrt(tok_rows * lax.axis_size(ALL))
    grad_term = (
        jnp.einsum("tbk,tbj->bkj", picked, chosen, preferred_element_type=jnp.float32) * grad_scale
    )
    delta_grad, full_weight = reduce_delta(grad_term, by_shard)

    block_term = jnp.einsum(
        "tbk,bkj->tbj", picked, delta_values, preferred_element_type=jnp.float32
    )
    sparse_part = (
        jnp.zeros((tok_rows, KVH * HD // BLK, BLK), jnp.float32)
        .at[:, col_index]
        .add(block_term)
        .reshape(tok_rows, KVH * HD)
    )
    dense_part = jnp.dot(tokens, full_weight, preferred_element_type=jnp.float32)
    values = (dense_part + sparse_part).astype(jnp.bfloat16)
    value_heads = values.reshape(tok_rows, KVH, HD)
    attention = (
        jnp.einsum("gstu,ugd->tgsd", attn_probs, value_heads, preferred_element_type=jnp.float32)
        .reshape(tok_rows, QH * HD)
        .astype(jnp.bfloat16)
    )
    dense_back = lax.dot_general(
        value_grad, full_weight, (((1,), (1,)), ((), ())), preferred_element_type=jnp.float32
    )
    back_term = jnp.einsum("tbj,bkj->tbk", chosen, delta_values, preferred_element_type=jnp.float32)
    spread_back = (
        jnp.zeros((tok_rows, D // BLK, BLK), jnp.float32)
        .at[:, row_index]
        .add(back_term)
        .reshape(tok_rows, D)
    )
    input_grad = (dense_back + spread_back).astype(jnp.bfloat16)
    return (attention, input_grad, delta_grad)


def solution(mesh):
    n_shard = mesh.shape["shard"]
    n_rep = mesh.shape["replica"]
    fine = Mesh(
        mesh.devices.reshape(2, 4, n_rep // 8, 4, n_shard // 4), ALL
    )
    tok = P(ALL, None)
    return jax.shard_map(
        local,
        mesh=fine,
        in_specs=(tok, tok, tok, tok, P(SHARD, None), P(), P(), tok),
        out_specs=(tok, tok, P(SHARD, None, None)),
        check_vma=False,
    )
```

```python
import math

import jax
import jax.numpy as jnp
from jax import lax
from jax.sharding import Mesh
from jax.sharding import PartitionSpec as P

D = 8192
QH = 64
KVH = 8
HD = 128
BLK = 64

REPLICA = ("zl", "x", "c")
SHARD = ("zh", "y")
ALL = REPLICA + SHARD
PIECE = ("x", "c")


def block_tables(block_list):
    row_hot = (block_list[:, 0:1] == jnp.arange(D // BLK, dtype=jnp.int32)[None, :]).astype(
        jnp.bfloat16
    )
    col_hot = (block_list[:, 1:2] == jnp.arange(KVH * HD // BLK, dtype=jnp.int32)[None, :]).astype(
        jnp.bfloat16
    )
    return (row_hot, col_hot)


def gather_pieces(base_weight):
    rows = base_weight.shape[0]
    pieces = lax.axis_size("x") * lax.axis_size("c")
    width = rows // pieces
    me = lax.axis_index("x") * lax.axis_size("c") + lax.axis_index("c")
    piece = lax.dynamic_slice_in_dim(base_weight, me * width, width, 0)
    return lax.all_gather(piece, SHARD, axis=0, tiled=False)


def gather_rest(by_shard):
    whole = lax.all_gather(by_shard, PIECE, axis=1, tiled=True)
    return whole.reshape(-1, whole.shape[-1])


def reduce_delta(grad_term):
    n_shard = lax.axis_size(SHARD)
    n_rep = lax.axis_size(REPLICA)
    nb = grad_term.shape[0]
    flat = grad_term.reshape(n_shard, -1)
    mine = lax.all_to_all(flat, SHARD, 0, 0, tiled=False).sum(0)
    mine = mine.reshape(n_rep, -1)
    part = lax.all_to_all(mine, REPLICA, 0, 0, tiled=False).sum(0)
    spread = jnp.broadcast_to(part[None], (n_rep,) + part.shape)
    whole = lax.all_to_all(spread, REPLICA, 0, 0, tiled=False)
    return whole.reshape(nb // n_shard, BLK, BLK)


def local(
    tokens,
    query_vectors,
    key_vectors,
    segment_ids,
    base_weight,
    delta_values,
    block_list,
    out_cotangent,
):
    tok_rows = tokens.shape[0]
    groups = QH // KVH
    row_index = block_list[:, 0]
    col_index = block_list[:, 1]
    by_shard = gather_pieces(base_weight)
    row_hot, col_hot = block_tables(block_list)
    picked = jnp.einsum(
        "trk,br->tbk",
        tokens.reshape(tok_rows, D // BLK, BLK),
        row_hot,
        preferred_element_type=jnp.float32,
    ).astype(jnp.bfloat16)
    query_heads = query_vectors.reshape(tok_rows, KVH, groups, HD)
    key_heads = key_vectors.reshape(tok_rows, KVH, HD)
    scores = jnp.einsum(
        "tgsd,ugd->gstu", query_heads, key_heads, preferred_element_type=jnp.float32
    ) * (1.0 / math.sqrt(HD))
    seg_row = segment_ids[0]
    position = jnp.arange(tok_rows, dtype=jnp.int32)
    allowed = (position[None, :] <= position[:, None]) & (seg_row[:, None] == seg_row[None, :])
    scores = jnp.where(allowed, scores, -1e30)
    row_max = jnp.max(scores, axis=-1, keepdims=True)
    exp_scores = jnp.exp(scores - row_max)
    attn_probs = (exp_scores / jnp.sum(exp_scores, axis=-1, keepdims=True)).astype(jnp.bfloat16)
    cotangent_heads = out_cotangent.reshape(tok_rows, KVH, groups, HD)
    value_grad = (
        jnp.einsum(
            "gstu,tgsd->ugd", attn_probs, cotangent_heads, preferred_element_type=jnp.float32
        )
        .reshape(tok_rows, KVH * HD)
        .astype(jnp.bfloat16)
    )
    chosen = jnp.einsum(
        "tcj,bc->tbj",
        value_grad.reshape(tok_rows, KVH * HD // BLK, BLK),
        col_hot,
        preferred_element_type=jnp.float32,
    ).astype(jnp.bfloat16)
    grad_scale = 1.0 / math.sqrt(tok_rows * lax.axis_size(ALL))
    grad_term = (
        jnp.einsum("tbk,tbj->bkj", picked, chosen, preferred_element_type=jnp.float32) * grad_scale
    )
    block_term = jnp.einsum(
        "tbk,bkj->tbj", picked, delta_values, preferred_element_type=jnp.float32
    )
    sparse_part = (
        jnp.zeros((tok_rows, KVH * HD // BLK, BLK), jnp.float32)
        .at[:, col_index]
        .add(block_term)
        .reshape(tok_rows, KVH * HD)
    )
    back_term = jnp.einsum("tbj,bkj->tbk", chosen, delta_values, preferred_element_type=jnp.float32)
    spread_back = (
        jnp.zeros((tok_rows, D // BLK, BLK), jnp.float32)
        .at[:, row_index]
        .add(back_term)
        .reshape(tok_rows, D)
    )
    by_shard, grad_term, sparse_part, spread_back = lax.optimization_barrier(
        (by_shard, grad_term, sparse_part, spread_back)
    )
    full_weight = gather_rest(by_shard)
    delta_grad = reduce_delta(grad_term)
    dense_part = jnp.dot(tokens, full_weight, preferred_element_type=jnp.float32)
    values = (dense_part + sparse_part).astype(jnp.bfloat16)
    value_heads = values.reshape(tok_rows, KVH, HD)
    attention = (
        jnp.einsum("gstu,ugd->tgsd", attn_probs, value_heads, preferred_element_type=jnp.float32)
        .reshape(tok_rows, QH * HD)
        .astype(jnp.bfloat16)
    )
    dense_back = lax.dot_general(
        value_grad, full_weight, (((1,), (1,)), ((), ())), preferred_element_type=jnp.float32
    )
    input_grad = (dense_back + spread_back).astype(jnp.bfloat16)
    return (attention, input_grad, delta_grad)


def solution(mesh):
    n_shard = mesh.shape["shard"]
    n_rep = mesh.shape["replica"]
    fine = Mesh(
        mesh.devices.reshape(2, 4, n_rep // 8, 4, n_shard // 4), ALL
    )
    tok = P(ALL, None)
    return jax.shard_map(
        local,
        mesh=fine,
        in_specs=(tok, tok, tok, tok, P(SHARD, None), P(), P(), tok),
        out_specs=(tok, tok, P(SHARD, None, None)),
        check_vma=False,
    )
```

```python
import math

import jax
import jax.numpy as jnp
from jax import lax
from jax.sharding import Mesh
from jax.sharding import PartitionSpec as P

D = 8192
QH = 64
KVH = 8
HD = 128
BLK = 64

REPLICA = ("zl", "x", "c")
SHARD = ("zh", "y")
ALL = REPLICA + SHARD
PIECE = ("x", "c")


def block_tables(block_list):
    row_hot = (block_list[:, 0:1] == jnp.arange(D // BLK, dtype=jnp.int32)[None, :]).astype(
        jnp.bfloat16
    )
    col_hot = (block_list[:, 1:2] == jnp.arange(KVH * HD // BLK, dtype=jnp.int32)[None, :]).astype(
        jnp.bfloat16
    )
    return (row_hot, col_hot)


def gather_pieces(base_weight):
    rows = base_weight.shape[0]
    pieces = lax.axis_size("x") * lax.axis_size("c")
    width = rows // pieces
    me = lax.axis_index("x") * lax.axis_size("c") + lax.axis_index("c")
    piece = lax.dynamic_slice_in_dim(base_weight, me * width, width, 0)
    return lax.all_gather(piece, SHARD, axis=0, tiled=False)


def gather_rest(by_shard):
    whole = lax.all_gather(by_shard, PIECE, axis=1, tiled=True)
    return whole.reshape(-1, whole.shape[-1])


def gather_halves(by_shard):
    half = by_shard.shape[0] // 2
    return gather_rest(by_shard[:half]), gather_rest(by_shard[half:])


def reduce_delta(grad_term):
    n_shard = lax.axis_size(SHARD)
    n_rep = lax.axis_size(REPLICA)
    nb = grad_term.shape[0]
    flat = grad_term.reshape(n_shard, -1)
    mine = lax.all_to_all(flat, SHARD, 0, 0, tiled=False).sum(0)
    mine = mine.reshape(n_rep, -1)
    part = lax.all_to_all(mine, REPLICA, 0, 0, tiled=False).sum(0)
    spread = jnp.broadcast_to(part[None], (n_rep,) + part.shape)
    whole = lax.all_to_all(spread, REPLICA, 0, 0, tiled=False)
    return whole.reshape(nb // n_shard, BLK, BLK)


def local(
    tokens,
    query_vectors,
    key_vectors,
    segment_ids,
    base_weight,
    delta_values,
    block_list,
    out_cotangent,
):
    tok_rows = tokens.shape[0]
    groups = QH // KVH
    row_index = block_list[:, 0]
    col_index = block_list[:, 1]
    by_shard = gather_pieces(base_weight)
    row_hot, col_hot = block_tables(block_list)
    picked = jnp.einsum(
        "trk,br->tbk",
        tokens.reshape(tok_rows, D // BLK, BLK),
        row_hot,
        preferred_element_type=jnp.float32,
    ).astype(jnp.bfloat16)
    query_heads = query_vectors.reshape(tok_rows, KVH, groups, HD)
    key_heads = key_vectors.reshape(tok_rows, KVH, HD)
    scores = jnp.einsum(
        "tgsd,ugd->gstu", query_heads, key_heads, preferred_element_type=jnp.float32
    ) * (1.0 / math.sqrt(HD))
    seg_row = segment_ids[0]
    position = jnp.arange(tok_rows, dtype=jnp.int32)
    allowed = (position[None, :] <= position[:, None]) & (seg_row[:, None] == seg_row[None, :])
    scores = jnp.where(allowed, scores, -1e30)
    row_max = jnp.max(scores, axis=-1, keepdims=True)
    exp_scores = jnp.exp(scores - row_max)
    attn_probs = (exp_scores / jnp.sum(exp_scores, axis=-1, keepdims=True)).astype(jnp.bfloat16)
    cotangent_heads = out_cotangent.reshape(tok_rows, KVH, groups, HD)
    value_grad = (
        jnp.einsum(
            "gstu,tgsd->ugd", attn_probs, cotangent_heads, preferred_element_type=jnp.float32
        )
        .reshape(tok_rows, KVH * HD)
        .astype(jnp.bfloat16)
    )
    chosen = jnp.einsum(
        "tcj,bc->tbj",
        value_grad.reshape(tok_rows, KVH * HD // BLK, BLK),
        col_hot,
        preferred_element_type=jnp.float32,
    ).astype(jnp.bfloat16)
    grad_scale = 1.0 / math.sqrt(tok_rows * lax.axis_size(ALL))
    grad_term = (
        jnp.einsum("tbk,tbj->bkj", picked, chosen, preferred_element_type=jnp.float32) * grad_scale
    )
    block_term = jnp.einsum(
        "tbk,bkj->tbj", picked, delta_values, preferred_element_type=jnp.float32
    )
    sparse_part = (
        jnp.zeros((tok_rows, KVH * HD // BLK, BLK), jnp.float32)
        .at[:, col_index]
        .add(block_term)
        .reshape(tok_rows, KVH * HD)
    )
    back_term = jnp.einsum("tbj,bkj->tbk", chosen, delta_values, preferred_element_type=jnp.float32)
    spread_back = (
        jnp.zeros((tok_rows, D // BLK, BLK), jnp.float32)
        .at[:, row_index]
        .add(back_term)
        .reshape(tok_rows, D)
    )
    by_shard, grad_term, sparse_part, spread_back = lax.optimization_barrier(
        (by_shard, grad_term, sparse_part, spread_back)
    )
    weight_a, weight_b = gather_halves(by_shard)
    split = weight_a.shape[0]
    delta_grad = reduce_delta(grad_term)
    dense_a = jnp.dot(tokens[:, :split], weight_a, preferred_element_type=jnp.float32)
    back_a = lax.dot_general(
        value_grad, weight_a, (((1,), (1,)), ((), ())), preferred_element_type=jnp.float32
    )
    dense_b = jnp.dot(tokens[:, split:], weight_b, preferred_element_type=jnp.float32)
    dense_part = dense_a + dense_b
    values = (dense_part + sparse_part).astype(jnp.bfloat16)
    value_heads = values.reshape(tok_rows, KVH, HD)
    attention = (
        jnp.einsum("gstu,ugd->tgsd", attn_probs, value_heads, preferred_element_type=jnp.float32)
        .reshape(tok_rows, QH * HD)
        .astype(jnp.bfloat16)
    )
    back_b = lax.dot_general(
        value_grad, weight_b, (((1,), (1,)), ((), ())), preferred_element_type=jnp.float32
    )
    dense_back = jnp.concatenate([back_a, back_b], axis=1)
    input_grad = (dense_back + spread_back).astype(jnp.bfloat16)
    return (attention, input_grad, delta_grad)


def solution(mesh):
    n_shard = mesh.shape["shard"]
    n_rep = mesh.shape["replica"]
    fine = Mesh(
        mesh.devices.reshape(2, 4, n_rep // 8, 4, n_shard // 4), ALL
    )
    tok = P(ALL, None)
    return jax.shard_map(
        local,
        mesh=fine,
        in_specs=(tok, tok, tok, tok, P(SHARD, None), P(), P(), tok),
        out_specs=(tok, tok, P(SHARD, None, None)),
        check_vma=False,
    )
```

```python
import math

import jax
import jax.numpy as jnp
from jax import lax
from jax.sharding import Mesh
from jax.sharding import PartitionSpec as P

D = 8192
QH = 64
KVH = 8
HD = 128
BLK = 64

REPLICA = ("zl", "x", "c")
SHARD = ("zh", "y")
ALL = REPLICA + SHARD


def block_tables(block_list):
    row_hot = (block_list[:, 0:1] == jnp.arange(D // BLK, dtype=jnp.int32)[None, :]).astype(
        jnp.bfloat16
    )
    col_hot = (block_list[:, 1:2] == jnp.arange(KVH * HD // BLK, dtype=jnp.int32)[None, :]).astype(
        jnp.bfloat16
    )
    return (row_hot, col_hot)


def gather_pieces(base_weight):
    width = base_weight.shape[0] // 2
    me = lax.axis_index("c")
    piece = lax.dynamic_slice_in_dim(base_weight, me * width, width, 0)
    return lax.all_gather(piece, SHARD, axis=0, tiled=False)


def half_products(tok4, value_grad, weight_half, half):
    tok_half = lax.dynamic_index_in_dim(tok4, half, 2, keepdims=False)
    dense = jnp.einsum("tsi,sin->tn", tok_half, weight_half, preferred_element_type=jnp.float32)
    back = jnp.einsum("tn,sin->tsi", value_grad, weight_half, preferred_element_type=jnp.float32)
    return dense, back


def reduce_delta(grad_term):
    n_shard = lax.axis_size(SHARD)
    n_rep = lax.axis_size(REPLICA)
    nb = grad_term.shape[0]
    flat = grad_term.reshape(n_shard, -1)
    mine = lax.all_to_all(flat, SHARD, 0, 0, tiled=False).sum(0)
    mine = mine.reshape(n_rep, -1)
    part = lax.all_to_all(mine, REPLICA, 0, 0, tiled=False).sum(0)
    spread = jnp.broadcast_to(part[None], (n_rep,) + part.shape)
    whole = lax.all_to_all(spread, REPLICA, 0, 0, tiled=False)
    return whole.reshape(nb // n_shard, BLK, BLK)


def local(
    tokens,
    query_vectors,
    key_vectors,
    segment_ids,
    base_weight,
    delta_values,
    block_list,
    out_cotangent,
):
    tok_rows = tokens.shape[0]
    groups = QH // KVH
    row_index = block_list[:, 0]
    col_index = block_list[:, 1]
    by_shard = gather_pieces(base_weight)
    row_hot, col_hot = block_tables(block_list)
    picked = jnp.einsum(
        "trk,br->tbk",
        tokens.reshape(tok_rows, D // BLK, BLK),
        row_hot,
        preferred_element_type=jnp.float32,
    ).astype(jnp.bfloat16)
    query_heads = query_vectors.reshape(tok_rows, KVH, groups, HD)
    key_heads = key_vectors.reshape(tok_rows, KVH, HD)
    scores = jnp.einsum(
        "tgsd,ugd->gstu", query_heads, key_heads, preferred_element_type=jnp.float32
    ) * (1.0 / math.sqrt(HD))
    seg_row = segment_ids[0]
    position = jnp.arange(tok_rows, dtype=jnp.int32)
    allowed = (position[None, :] <= position[:, None]) & (seg_row[:, None] == seg_row[None, :])
    scores = jnp.where(allowed, scores, -1e30)
    row_max = jnp.max(scores, axis=-1, keepdims=True)
    exp_scores = jnp.exp(scores - row_max)
    attn_probs = (exp_scores / jnp.sum(exp_scores, axis=-1, keepdims=True)).astype(jnp.bfloat16)
    cotangent_heads = out_cotangent.reshape(tok_rows, KVH, groups, HD)
    value_grad = (
        jnp.einsum(
            "gstu,tgsd->ugd", attn_probs, cotangent_heads, preferred_element_type=jnp.float32
        )
        .reshape(tok_rows, KVH * HD)
        .astype(jnp.bfloat16)
    )
    chosen = jnp.einsum(
        "tcj,bc->tbj",
        value_grad.reshape(tok_rows, KVH * HD // BLK, BLK),
        col_hot,
        preferred_element_type=jnp.float32,
    ).astype(jnp.bfloat16)
    grad_scale = 1.0 / math.sqrt(tok_rows * lax.axis_size(ALL))
    grad_term = (
        jnp.einsum("tbk,tbj->bkj", picked, chosen, preferred_element_type=jnp.float32) * grad_scale
    )
    block_term = jnp.einsum(
        "tbk,bkj->tbj", picked, delta_values, preferred_element_type=jnp.float32
    )
    sparse_part = (
        jnp.zeros((tok_rows, KVH * HD // BLK, BLK), jnp.float32)
        .at[:, col_index]
        .add(block_term)
        .reshape(tok_rows, KVH * HD)
    )
    back_term = jnp.einsum("tbj,bkj->tbk", chosen, delta_values, preferred_element_type=jnp.float32)
    spread_back = (
        jnp.zeros((tok_rows, D // BLK, BLK), jnp.float32)
        .at[:, row_index]
        .add(back_term)
        .reshape(tok_rows, D)
    )
    delta_grad = reduce_delta(grad_term)
    by_shard, delta_grad, sparse_part, spread_back = lax.optimization_barrier(
        (by_shard, delta_grad, sparse_part, spread_back)
    )
    other = lax.ppermute(by_shard, "c", [(0, 1), (1, 0)])
    me = lax.axis_index("c")
    n_shard = by_shard.shape[0]
    tok4 = tokens.reshape(tok_rows, n_shard, 2, -1)
    dense_own, back_own = half_products(tok4, value_grad, by_shard, me)
    dense_other, back_other = half_products(tok4, value_grad, other, 1 - me)
    dense_part = dense_own + dense_other
    is_own = lax.broadcasted_iota(jnp.int32, tok4.shape, 2) == me
    back4 = jnp.where(is_own, back_own[:, :, None, :], back_other[:, :, None, :])
    dense_back = back4.reshape(tok_rows, D)
    values = (dense_part + sparse_part).astype(jnp.bfloat16)
    value_heads = values.reshape(tok_rows, KVH, HD)
    attention = (
        jnp.einsum("gstu,ugd->tgsd", attn_probs, value_heads, preferred_element_type=jnp.float32)
        .reshape(tok_rows, QH * HD)
        .astype(jnp.bfloat16)
    )
    input_grad = (dense_back + spread_back).astype(jnp.bfloat16)
    return (attention, input_grad, delta_grad)


def solution(mesh):
    n_shard = mesh.shape["shard"]
    n_rep = mesh.shape["replica"]
    fine = Mesh(
        mesh.devices.reshape(2, 4, n_rep // 8, 4, n_shard // 4), ALL
    )
    tok = P(ALL, None)
    return jax.shard_map(
        local,
        mesh=fine,
        in_specs=(tok, tok, tok, tok, P(SHARD, None), P(), P(), tok),
        out_specs=(tok, tok, P(SHARD, None, None)),
        check_vma=False,
    )
```

```python
import math

import jax
import jax.numpy as jnp
from jax import lax
from jax.sharding import Mesh
from jax.sharding import PartitionSpec as P

D = 8192
QH = 64
KVH = 8
HD = 128
BLK = 64

REPLICA = ("zl", "x", "c")
SHARD = ("zh", "y")
ALL = REPLICA + SHARD
PIECE = ("x", "c")


def block_tables(block_list):
    row_hot = (block_list[:, 0:1] == jnp.arange(D // BLK, dtype=jnp.int32)[None, :]).astype(
        jnp.bfloat16
    )
    col_hot = (block_list[:, 1:2] == jnp.arange(KVH * HD // BLK, dtype=jnp.int32)[None, :]).astype(
        jnp.bfloat16
    )
    return (row_hot, col_hot)


def gather_pieces(base_weight):
    rows = base_weight.shape[0]
    pieces = lax.axis_size("x") * lax.axis_size("c")
    width = rows // pieces
    me = lax.axis_index("x") * lax.axis_size("c") + lax.axis_index("c")
    piece = lax.dynamic_slice_in_dim(base_weight, me * width, width, 0)
    return lax.all_gather(piece, SHARD, axis=0, tiled=False)


def piece_index():
    return lax.axis_index("x") * lax.axis_size("c") + lax.axis_index("c")


def gather_rest(by_shard):
    pieces = lax.axis_size("x") * lax.axis_size("c")
    got = [by_shard]
    for k in range(1, pieces):
        got.append(lax.ppermute(by_shard, PIECE, [(j, (j + k) % pieces) for j in range(pieces)]))
    return got


def to_slots(arr, me):
    pieces = arr.shape[2]
    twice = jnp.concatenate([arr, arr], axis=2)
    rolled = lax.dynamic_slice_in_dim(twice, me + 1, pieces, 2)
    return rolled[:, :, ::-1]


def from_slots(arr, me):
    pieces = arr.shape[2]
    flipped = arr[:, :, ::-1]
    twice = jnp.concatenate([flipped, flipped], axis=2)
    return lax.dynamic_slice_in_dim(twice, pieces - 1 - me, pieces, 2)


def reduce_delta(grad_term):
    n_shard = lax.axis_size(SHARD)
    n_rep = lax.axis_size(REPLICA)
    nb = grad_term.shape[0]
    flat = grad_term.reshape(n_shard, -1)
    mine = lax.all_to_all(flat, SHARD, 0, 0, tiled=False).sum(0)
    mine = mine.reshape(n_rep, -1)
    part = lax.all_to_all(mine, REPLICA, 0, 0, tiled=False).sum(0)
    spread = jnp.broadcast_to(part[None], (n_rep,) + part.shape)
    whole = lax.all_to_all(spread, REPLICA, 0, 0, tiled=False)
    return whole.reshape(nb // n_shard, BLK, BLK)


def local(
    tokens,
    query_vectors,
    key_vectors,
    segment_ids,
    base_weight,
    delta_values,
    block_list,
    out_cotangent,
):
    tok_rows = tokens.shape[0]
    groups = QH // KVH
    row_index = block_list[:, 0]
    col_index = block_list[:, 1]
    by_shard = gather_pieces(base_weight)
    row_hot, col_hot = block_tables(block_list)
    picked = jnp.einsum(
        "trk,br->tbk",
        tokens.reshape(tok_rows, D // BLK, BLK),
        row_hot,
        preferred_element_type=jnp.float32,
    ).astype(jnp.bfloat16)
    query_heads = query_vectors.reshape(tok_rows, KVH, groups, HD)
    key_heads = key_vectors.reshape(tok_rows, KVH, HD)
    scores = jnp.einsum(
        "tgsd,ugd->gstu", query_heads, key_heads, preferred_element_type=jnp.float32
    ) * (1.0 / math.sqrt(HD))
    seg_row = segment_ids[0]
    position = jnp.arange(tok_rows, dtype=jnp.int32)
    allowed = (position[None, :] <= position[:, None]) & (seg_row[:, None] == seg_row[None, :])
    scores = jnp.where(allowed, scores, -1e30)
    row_max = jnp.max(scores, axis=-1, keepdims=True)
    exp_scores = jnp.exp(scores - row_max)
    attn_probs = (exp_scores / jnp.sum(exp_scores, axis=-1, keepdims=True)).astype(jnp.bfloat16)
    cotangent_heads = out_cotangent.reshape(tok_rows, KVH, groups, HD)
    value_grad = (
        jnp.einsum(
            "gstu,tgsd->ugd", attn_probs, cotangent_heads, preferred_element_type=jnp.float32
        )
        .reshape(tok_rows, KVH * HD)
        .astype(jnp.bfloat16)
    )
    chosen = jnp.einsum(
        "tcj,bc->tbj",
        value_grad.reshape(tok_rows, KVH * HD // BLK, BLK),
        col_hot,
        preferred_element_type=jnp.float32,
    ).astype(jnp.bfloat16)
    grad_scale = 1.0 / math.sqrt(tok_rows * lax.axis_size(ALL))
    grad_term = (
        jnp.einsum("tbk,tbj->bkj", picked, chosen, preferred_element_type=jnp.float32) * grad_scale
    )
    block_term = jnp.einsum(
        "tbk,bkj->tbj", picked, delta_values, preferred_element_type=jnp.float32
    )
    sparse_part = (
        jnp.zeros((tok_rows, KVH * HD // BLK, BLK), jnp.float32)
        .at[:, col_index]
        .add(block_term)
        .reshape(tok_rows, KVH * HD)
    )
    back_term = jnp.einsum("tbj,bkj->tbk", chosen, delta_values, preferred_element_type=jnp.float32)
    spread_back = (
        jnp.zeros((tok_rows, D // BLK, BLK), jnp.float32)
        .at[:, row_index]
        .add(back_term)
        .reshape(tok_rows, D)
    )
    by_shard, grad_term, sparse_part, spread_back = lax.optimization_barrier(
        (by_shard, grad_term, sparse_part, spread_back)
    )
    got = gather_rest(by_shard)
    delta_grad = reduce_delta(grad_term)
    me = piece_index()
    n_shard, width = by_shard.shape[0], by_shard.shape[1]
    tok_slots = to_slots(tokens.reshape(tok_rows, n_shard, len(got), width), me)
    dense_part = None
    backs = []
    for k, piece in enumerate(got):
        part = jnp.einsum(
            "tsi,sin->tn", tok_slots[:, :, k], piece, preferred_element_type=jnp.float32
        )
        dense_part = part if dense_part is None else dense_part + part
        backs.append(
            jnp.einsum("tn,sin->tsi", value_grad, piece, preferred_element_type=jnp.float32)
        )
    dense_back = from_slots(jnp.stack(backs, axis=2), me).reshape(tok_rows, D)
    values = (dense_part + sparse_part).astype(jnp.bfloat16)
    value_heads = values.reshape(tok_rows, KVH, HD)
    attention = (
        jnp.einsum("gstu,ugd->tgsd", attn_probs, value_heads, preferred_element_type=jnp.float32)
        .reshape(tok_rows, QH * HD)
        .astype(jnp.bfloat16)
    )
    input_grad = (dense_back + spread_back).astype(jnp.bfloat16)
    return (attention, input_grad, delta_grad)


def solution(mesh):
    n_shard = mesh.shape["shard"]
    n_rep = mesh.shape["replica"]
    fine = Mesh(
        mesh.devices.reshape(2, 4, n_rep // 8, 4, n_shard // 4), ALL
    )
    tok = P(ALL, None)
    return jax.shard_map(
        local,
        mesh=fine,
        in_specs=(tok, tok, tok, tok, P(SHARD, None), P(), P(), tok),
        out_specs=(tok, tok, P(SHARD, None, None)),
        check_vma=False,
    )
```

```python
import math

import jax
import jax.numpy as jnp
from jax import lax
from jax.experimental import pallas as pl
from jax.experimental.pallas import tpu as pltpu
from jax.sharding import Mesh
from jax.sharding import PartitionSpec as P

D = 8192
QH = 64
KVH = 8
HD = 128
BLK = 64

REPLICA = ("zl", "x", "c")
SHARD = ("zh", "y")
ALL = REPLICA + SHARD
PIECE = ("x", "c")


def block_tables(block_list):
    row_hot = (block_list[:, 0:1] == jnp.arange(D // BLK, dtype=jnp.int32)[None, :]).astype(
        jnp.bfloat16
    )
    col_hot = (block_list[:, 1:2] == jnp.arange(KVH * HD // BLK, dtype=jnp.int32)[None, :]).astype(
        jnp.bfloat16
    )
    return (row_hot, col_hot)


def gather_pieces(base_weight):
    rows = base_weight.shape[0]
    pieces = lax.axis_size("x") * lax.axis_size("c")
    width = rows // pieces
    me = lax.axis_index("x") * lax.axis_size("c") + lax.axis_index("c")
    piece = lax.dynamic_slice_in_dim(base_weight, me * width, width, 0)
    return lax.all_gather(piece, SHARD, axis=0, tiled=False)


def gather_rest(by_shard):
    whole = lax.all_gather(by_shard, PIECE, axis=1, tiled=True)
    return whole.reshape(-1, whole.shape[-1])


def tail_kernel(tok_ref, w_ref, vg_ref, sb_ref, sp_ref, val_ref, ig_ref, acc_ref):
    k = pl.program_id(0)

    @pl.when(k == 0)
    def _():
        acc_ref[...] = sp_ref[...]

    w = w_ref[...]
    acc_ref[...] += jnp.dot(tok_ref[...], w, preferred_element_type=jnp.float32)
    back = lax.dot_general(
        vg_ref[...], w, (((1,), (1,)), ((), ())), preferred_element_type=jnp.float32
    )
    ig_ref[...] = (back + sb_ref[...]).astype(ig_ref.dtype)

    @pl.when(k == pl.num_programs(0) - 1)
    def _():
        val_ref[...] = acc_ref[...].astype(val_ref.dtype)


def dense_tail(tokens, full_weight, value_grad, spread_back, sparse_part):
    rows, depth = tokens.shape
    width = full_weight.shape[1]
    tile = 512
    steps = depth // tile
    return pl.pallas_call(
        tail_kernel,
        grid=(steps,),
        in_specs=[
            pl.BlockSpec((rows, tile), lambda k: (0, k)),
            pl.BlockSpec((tile, width), lambda k: (k, 0)),
            pl.BlockSpec((rows, width), lambda k: (0, 0)),
            pl.BlockSpec((rows, tile), lambda k: (0, k)),
            pl.BlockSpec((rows, width), lambda k: (0, 0)),
        ],
        out_specs=[
            pl.BlockSpec((rows, width), lambda k: (0, 0)),
            pl.BlockSpec((rows, tile), lambda k: (0, k)),
        ],
        out_shape=[
            jax.ShapeDtypeStruct((rows, width), jnp.bfloat16),
            jax.ShapeDtypeStruct((rows, depth), jnp.bfloat16),
        ],
        scratch_shapes=[pltpu.VMEM((rows, width), jnp.float32)],
        compiler_params=pltpu.CompilerParams(dimension_semantics=("arbitrary",)),
        cost_estimate=pl.CostEstimate(
            flops=4 * rows * depth * width,
            bytes_accessed=2 * depth * width + 8 * rows * depth + 10 * rows * width,
            transcendentals=0,
        ),
    )(tokens, full_weight, value_grad, spread_back, sparse_part)


def reduce_delta(grad_term):
    n_shard = lax.axis_size(SHARD)
    n_rep = lax.axis_size(REPLICA)
    nb = grad_term.shape[0]
    flat = grad_term.reshape(n_shard, -1)
    mine = lax.all_to_all(flat, SHARD, 0, 0, tiled=False).sum(0)
    mine = mine.reshape(n_rep, -1)
    part = lax.all_to_all(mine, REPLICA, 0, 0, tiled=False).sum(0)
    spread = jnp.broadcast_to(part[None], (n_rep,) + part.shape)
    whole = lax.all_to_all(spread, REPLICA, 0, 0, tiled=False)
    return whole.reshape(nb // n_shard, BLK, BLK)


def local(
    tokens,
    query_vectors,
    key_vectors,
    segment_ids,
    base_weight,
    delta_values,
    block_list,
    out_cotangent,
):
    tok_rows = tokens.shape[0]
    groups = QH // KVH
    row_index = block_list[:, 0]
    col_index = block_list[:, 1]
    by_shard = gather_pieces(base_weight)
    row_hot, col_hot = block_tables(block_list)
    picked = jnp.einsum(
        "trk,br->tbk",
        tokens.reshape(tok_rows, D // BLK, BLK),
        row_hot,
        preferred_element_type=jnp.float32,
    ).astype(jnp.bfloat16)
    query_heads = query_vectors.reshape(tok_rows, KVH, groups, HD)
    key_heads = key_vectors.reshape(tok_rows, KVH, HD)
    scores = jnp.einsum(
        "tgsd,ugd->gstu", query_heads, key_heads, preferred_element_type=jnp.float32
    ) * (1.0 / math.sqrt(HD))
    seg_row = segment_ids[0]
    position = jnp.arange(tok_rows, dtype=jnp.int32)
    allowed = (position[None, :] <= position[:, None]) & (seg_row[:, None] == seg_row[None, :])
    scores = jnp.where(allowed, scores, -1e30)
    row_max = jnp.max(scores, axis=-1, keepdims=True)
    exp_scores = jnp.exp(scores - row_max)
    attn_probs = (exp_scores / jnp.sum(exp_scores, axis=-1, keepdims=True)).astype(jnp.bfloat16)
    cotangent_heads = out_cotangent.reshape(tok_rows, KVH, groups, HD)
    value_grad = (
        jnp.einsum(
            "gstu,tgsd->ugd", attn_probs, cotangent_heads, preferred_element_type=jnp.float32
        )
        .reshape(tok_rows, KVH * HD)
        .astype(jnp.bfloat16)
    )
    chosen = jnp.einsum(
        "tcj,bc->tbj",
        value_grad.reshape(tok_rows, KVH * HD // BLK, BLK),
        col_hot,
        preferred_element_type=jnp.float32,
    ).astype(jnp.bfloat16)
    grad_scale = 1.0 / math.sqrt(tok_rows * lax.axis_size(ALL))
    grad_term = (
        jnp.einsum("tbk,tbj->bkj", picked, chosen, preferred_element_type=jnp.float32) * grad_scale
    )
    block_term = jnp.einsum(
        "tbk,bkj->tbj", picked, delta_values, preferred_element_type=jnp.float32
    )
    sparse_part = (
        jnp.zeros((tok_rows, KVH * HD // BLK, BLK), jnp.float32)
        .at[:, col_index]
        .add(block_term)
        .reshape(tok_rows, KVH * HD)
    )
    back_term = jnp.einsum("tbj,bkj->tbk", chosen, delta_values, preferred_element_type=jnp.float32)
    spread_back = (
        jnp.zeros((tok_rows, D // BLK, BLK), jnp.float32)
        .at[:, row_index]
        .add(back_term)
        .reshape(tok_rows, D)
    )
    by_shard, grad_term, sparse_part, spread_back = lax.optimization_barrier(
        (by_shard, grad_term, sparse_part, spread_back)
    )
    full_weight = gather_rest(by_shard)
    delta_grad = reduce_delta(grad_term)
    values, input_grad = dense_tail(tokens, full_weight, value_grad, spread_back, sparse_part)
    value_heads = values.reshape(tok_rows, KVH, HD)
    attention = (
        jnp.einsum("gstu,ugd->tgsd", attn_probs, value_heads, preferred_element_type=jnp.float32)
        .reshape(tok_rows, QH * HD)
        .astype(jnp.bfloat16)
    )
    return (attention, input_grad, delta_grad)


def solution(mesh):
    n_shard = mesh.shape["shard"]
    n_rep = mesh.shape["replica"]
    fine = Mesh(
        mesh.devices.reshape(2, 4, n_rep // 8, 4, n_shard // 4), ALL
    )
    tok = P(ALL, None)
    return jax.shard_map(
        local,
        mesh=fine,
        in_specs=(tok, tok, tok, tok, P(SHARD, None), P(), P(), tok),
        out_specs=(tok, tok, P(SHARD, None, None)),
        check_vma=False,
    )
```

```python
import math

import jax
import jax.numpy as jnp
from jax import lax
from jax.experimental import pallas as pl
from jax.experimental.pallas import tpu as pltpu
from jax.sharding import Mesh
from jax.sharding import PartitionSpec as P

D = 8192
QH = 64
KVH = 8
HD = 128
BLK = 64

REPLICA = ("zl", "x", "c")
SHARD = ("zh", "y")
ALL = REPLICA + SHARD
PIECE = ("x", "c")


def block_tables(block_list):
    row_hot = (block_list[:, 0:1] == jnp.arange(D // BLK, dtype=jnp.int32)[None, :]).astype(
        jnp.bfloat16
    )
    col_hot = (block_list[:, 1:2] == jnp.arange(KVH * HD // BLK, dtype=jnp.int32)[None, :]).astype(
        jnp.bfloat16
    )
    return (row_hot, col_hot)


def gather_pieces(base_weight):
    rows = base_weight.shape[0]
    pieces = lax.axis_size("x") * lax.axis_size("c")
    width = rows // pieces
    me = lax.axis_index("x") * lax.axis_size("c") + lax.axis_index("c")
    piece = lax.dynamic_slice_in_dim(base_weight, me * width, width, 0)
    return lax.all_gather(piece, SHARD, axis=0, tiled=False)


def gather_rest(by_shard):
    whole = lax.all_gather(by_shard, PIECE, axis=1, tiled=True)
    return whole.reshape(-1, whole.shape[-1])


def tail_kernel(tok_ref, w_ref, vg_ref, sb_ref, sp_ref, val_ref, ig_ref, acc_ref):
    k = pl.program_id(0)

    @pl.when(k == 0)
    def _():
        acc_ref[...] = sp_ref[...]

    w = w_ref[...]
    acc_ref[...] += jnp.dot(tok_ref[...], w, preferred_element_type=jnp.float32)
    back = lax.dot_general(
        vg_ref[...], w, (((1,), (1,)), ((), ())), preferred_element_type=jnp.float32
    )
    ig_ref[...] = (back + sb_ref[...]).astype(ig_ref.dtype)

    @pl.when(k == pl.num_programs(0) - 1)
    def _():
        val_ref[...] = acc_ref[...].astype(val_ref.dtype)


def dense_tail(tokens, full_weight, value_grad, spread_back, sparse_part):
    rows, depth = tokens.shape
    width = full_weight.shape[1]
    tile = 1024
    steps = depth // tile
    return pl.pallas_call(
        tail_kernel,
        grid=(steps,),
        in_specs=[
            pl.BlockSpec((rows, tile), lambda k: (0, k)),
            pl.BlockSpec((tile, width), lambda k: (k, 0)),
            pl.BlockSpec((rows, width), lambda k: (0, 0)),
            pl.BlockSpec((rows, tile), lambda k: (0, k)),
            pl.BlockSpec((rows, width), lambda k: (0, 0)),
        ],
        out_specs=[
            pl.BlockSpec((rows, width), lambda k: (0, 0)),
            pl.BlockSpec((rows, tile), lambda k: (0, k)),
        ],
        out_shape=[
            jax.ShapeDtypeStruct((rows, width), jnp.bfloat16),
            jax.ShapeDtypeStruct((rows, depth), jnp.bfloat16),
        ],
        scratch_shapes=[pltpu.VMEM((rows, width), jnp.float32)],
        compiler_params=pltpu.CompilerParams(dimension_semantics=("arbitrary",)),
        cost_estimate=pl.CostEstimate(
            flops=4 * rows * depth * width,
            bytes_accessed=2 * depth * width + 8 * rows * depth + 10 * rows * width,
            transcendentals=0,
        ),
    )(tokens, full_weight, value_grad, spread_back, sparse_part)


def reduce_delta(grad_term):
    n_shard = lax.axis_size(SHARD)
    n_rep = lax.axis_size(REPLICA)
    nb = grad_term.shape[0]
    flat = grad_term.reshape(n_shard, -1)
    mine = lax.all_to_all(flat, SHARD, 0, 0, tiled=False).sum(0)
    mine = mine.reshape(n_rep, -1)
    part = lax.all_to_all(mine, REPLICA, 0, 0, tiled=False).sum(0)
    spread = jnp.broadcast_to(part[None], (n_rep,) + part.shape)
    whole = lax.all_to_all(spread, REPLICA, 0, 0, tiled=False)
    return whole.reshape(nb // n_shard, BLK, BLK)


def local(
    tokens,
    query_vectors,
    key_vectors,
    segment_ids,
    base_weight,
    delta_values,
    block_list,
    out_cotangent,
):
    tok_rows = tokens.shape[0]
    groups = QH // KVH
    row_index = block_list[:, 0]
    col_index = block_list[:, 1]
    by_shard = gather_pieces(base_weight)
    row_hot, col_hot = block_tables(block_list)
    picked = jnp.einsum(
        "trk,br->tbk",
        tokens.reshape(tok_rows, D // BLK, BLK),
        row_hot,
        preferred_element_type=jnp.float32,
    ).astype(jnp.bfloat16)
    query_heads = query_vectors.reshape(tok_rows, KVH, groups, HD)
    key_heads = key_vectors.reshape(tok_rows, KVH, HD)
    scores = jnp.einsum(
        "tgsd,ugd->gstu", query_heads, key_heads, preferred_element_type=jnp.float32
    ) * (1.0 / math.sqrt(HD))
    seg_row = segment_ids[0]
    position = jnp.arange(tok_rows, dtype=jnp.int32)
    allowed = (position[None, :] <= position[:, None]) & (seg_row[:, None] == seg_row[None, :])
    scores = jnp.where(allowed, scores, -1e30)
    row_max = jnp.max(scores, axis=-1, keepdims=True)
    exp_scores = jnp.exp(scores - row_max)
    attn_probs = (exp_scores / jnp.sum(exp_scores, axis=-1, keepdims=True)).astype(jnp.bfloat16)
    cotangent_heads = out_cotangent.reshape(tok_rows, KVH, groups, HD)
    value_grad = (
        jnp.einsum(
            "gstu,tgsd->ugd", attn_probs, cotangent_heads, preferred_element_type=jnp.float32
        )
        .reshape(tok_rows, KVH * HD)
        .astype(jnp.bfloat16)
    )
    chosen = jnp.einsum(
        "tcj,bc->tbj",
        value_grad.reshape(tok_rows, KVH * HD // BLK, BLK),
        col_hot,
        preferred_element_type=jnp.float32,
    ).astype(jnp.bfloat16)
    grad_scale = 1.0 / math.sqrt(tok_rows * lax.axis_size(ALL))
    grad_term = (
        jnp.einsum("tbk,tbj->bkj", picked, chosen, preferred_element_type=jnp.float32) * grad_scale
    )
    block_term = jnp.einsum(
        "tbk,bkj->tbj", picked, delta_values, preferred_element_type=jnp.float32
    )
    sparse_part = (
        jnp.zeros((tok_rows, KVH * HD // BLK, BLK), jnp.float32)
        .at[:, col_index]
        .add(block_term)
        .reshape(tok_rows, KVH * HD)
    )
    back_term = jnp.einsum("tbj,bkj->tbk", chosen, delta_values, preferred_element_type=jnp.float32)
    spread_back = (
        jnp.zeros((tok_rows, D // BLK, BLK), jnp.float32)
        .at[:, row_index]
        .add(back_term)
        .reshape(tok_rows, D)
    )
    by_shard, grad_term, sparse_part, spread_back = lax.optimization_barrier(
        (by_shard, grad_term, sparse_part, spread_back)
    )
    full_weight = gather_rest(by_shard)
    delta_grad = reduce_delta(grad_term)
    values, input_grad = dense_tail(tokens, full_weight, value_grad, spread_back, sparse_part)
    value_heads = values.reshape(tok_rows, KVH, HD)
    attention = (
        jnp.einsum("gstu,ugd->tgsd", attn_probs, value_heads, preferred_element_type=jnp.float32)
        .reshape(tok_rows, QH * HD)
        .astype(jnp.bfloat16)
    )
    return (attention, input_grad, delta_grad)


def solution(mesh):
    n_shard = mesh.shape["shard"]
    n_rep = mesh.shape["replica"]
    fine = Mesh(
        mesh.devices.reshape(2, 4, n_rep // 8, 4, n_shard // 4), ALL
    )
    tok = P(ALL, None)
    return jax.shard_map(
        local,
        mesh=fine,
        in_specs=(tok, tok, tok, tok, P(SHARD, None), P(), P(), tok),
        out_specs=(tok, tok, P(SHARD, None, None)),
        check_vma=False,
    )
```

```python
import math

import jax
import jax.numpy as jnp
from jax import lax
from jax.experimental import pallas as pl
from jax.experimental.pallas import tpu as pltpu
from jax.sharding import Mesh
from jax.sharding import PartitionSpec as P

D = 8192
QH = 64
KVH = 8
HD = 128
BLK = 64

REPLICA = ("zl", "x", "c")
SHARD = ("zh", "y")
ALL = REPLICA + SHARD
PIECE = ("x", "c")


def block_tables(block_list):
    row_hot = (block_list[:, 0:1] == jnp.arange(D // BLK, dtype=jnp.int32)[None, :]).astype(
        jnp.bfloat16
    )
    col_hot = (block_list[:, 1:2] == jnp.arange(KVH * HD // BLK, dtype=jnp.int32)[None, :]).astype(
        jnp.bfloat16
    )
    return (row_hot, col_hot)


def gather_pieces(base_weight):
    rows = base_weight.shape[0]
    pieces = lax.axis_size("x") * lax.axis_size("c")
    width = rows // pieces
    me = lax.axis_index("x") * lax.axis_size("c") + lax.axis_index("c")
    piece = lax.dynamic_slice_in_dim(base_weight, me * width, width, 0)
    return lax.all_gather(piece, SHARD, axis=0, tiled=False)


def gather_rest(by_shard):
    whole = lax.all_gather(by_shard, PIECE, axis=1, tiled=True)
    return whole.reshape(-1, whole.shape[-1])


def tail_kernel(tok_ref, w_ref, vg_ref, sb_ref, sp_ref, val_ref, ig_ref, acc_ref):
    k = pl.program_id(0)

    @pl.when(k == 0)
    def _():
        acc_ref[...] = sp_ref[...]

    w = w_ref[...]
    acc_ref[...] += jnp.dot(tok_ref[...], w, preferred_element_type=jnp.float32)
    back = lax.dot_general(
        vg_ref[...], w, (((1,), (1,)), ((), ())), preferred_element_type=jnp.float32
    )
    ig_ref[...] = (back + sb_ref[...]).astype(ig_ref.dtype)

    @pl.when(k == pl.num_programs(0) - 1)
    def _():
        val_ref[...] = acc_ref[...].astype(val_ref.dtype)


def dense_tail(tokens, full_weight, value_grad, spread_back, sparse_part):
    rows, depth = tokens.shape
    width = full_weight.shape[1]
    tile = 2048
    steps = depth // tile
    return pl.pallas_call(
        tail_kernel,
        grid=(steps,),
        in_specs=[
            pl.BlockSpec((rows, tile), lambda k: (0, k)),
            pl.BlockSpec((tile, width), lambda k: (k, 0)),
            pl.BlockSpec((rows, width), lambda k: (0, 0)),
            pl.BlockSpec((rows, tile), lambda k: (0, k)),
            pl.BlockSpec((rows, width), lambda k: (0, 0)),
        ],
        out_specs=[
            pl.BlockSpec((rows, width), lambda k: (0, 0)),
            pl.BlockSpec((rows, tile), lambda k: (0, k)),
        ],
        out_shape=[
            jax.ShapeDtypeStruct((rows, width), jnp.bfloat16),
            jax.ShapeDtypeStruct((rows, depth), jnp.bfloat16),
        ],
        scratch_shapes=[pltpu.VMEM((rows, width), jnp.float32)],
        compiler_params=pltpu.CompilerParams(dimension_semantics=("arbitrary",)),
        cost_estimate=pl.CostEstimate(
            flops=4 * rows * depth * width,
            bytes_accessed=2 * depth * width + 8 * rows * depth + 10 * rows * width,
            transcendentals=0,
        ),
    )(tokens, full_weight, value_grad, spread_back, sparse_part)


def reduce_delta(grad_term):
    n_shard = lax.axis_size(SHARD)
    n_rep = lax.axis_size(REPLICA)
    nb = grad_term.shape[0]
    flat = grad_term.reshape(n_shard, -1)
    mine = lax.all_to_all(flat, SHARD, 0, 0, tiled=False).sum(0)
    mine = mine.reshape(n_rep, -1)
    part = lax.all_to_all(mine, REPLICA, 0, 0, tiled=False).sum(0)
    spread = jnp.broadcast_to(part[None], (n_rep,) + part.shape)
    whole = lax.all_to_all(spread, REPLICA, 0, 0, tiled=False)
    return whole.reshape(nb // n_shard, BLK, BLK)


def local(
    tokens,
    query_vectors,
    key_vectors,
    segment_ids,
    base_weight,
    delta_values,
    block_list,
    out_cotangent,
):
    tok_rows = tokens.shape[0]
    groups = QH // KVH
    row_index = block_list[:, 0]
    col_index = block_list[:, 1]
    by_shard = gather_pieces(base_weight)
    row_hot, col_hot = block_tables(block_list)
    picked = jnp.einsum(
        "trk,br->tbk",
        tokens.reshape(tok_rows, D // BLK, BLK),
        row_hot,
        preferred_element_type=jnp.float32,
    ).astype(jnp.bfloat16)
    query_heads = query_vectors.reshape(tok_rows, KVH, groups, HD)
    key_heads = key_vectors.reshape(tok_rows, KVH, HD)
    scores = jnp.einsum(
        "tgsd,ugd->gstu", query_heads, key_heads, preferred_element_type=jnp.float32
    ) * (1.0 / math.sqrt(HD))
    seg_row = segment_ids[0]
    position = jnp.arange(tok_rows, dtype=jnp.int32)
    allowed = (position[None, :] <= position[:, None]) & (seg_row[:, None] == seg_row[None, :])
    scores = jnp.where(allowed, scores, -1e30)
    row_max = jnp.max(scores, axis=-1, keepdims=True)
    exp_scores = jnp.exp(scores - row_max)
    attn_probs = (exp_scores / jnp.sum(exp_scores, axis=-1, keepdims=True)).astype(jnp.bfloat16)
    cotangent_heads = out_cotangent.reshape(tok_rows, KVH, groups, HD)
    value_grad = (
        jnp.einsum(
            "gstu,tgsd->ugd", attn_probs, cotangent_heads, preferred_element_type=jnp.float32
        )
        .reshape(tok_rows, KVH * HD)
        .astype(jnp.bfloat16)
    )
    chosen = jnp.einsum(
        "tcj,bc->tbj",
        value_grad.reshape(tok_rows, KVH * HD // BLK, BLK),
        col_hot,
        preferred_element_type=jnp.float32,
    ).astype(jnp.bfloat16)
    grad_scale = 1.0 / math.sqrt(tok_rows * lax.axis_size(ALL))
    grad_term = (
        jnp.einsum("tbk,tbj->bkj", picked, chosen, preferred_element_type=jnp.float32) * grad_scale
    )
    block_term = jnp.einsum(
        "tbk,bkj->tbj", picked, delta_values, preferred_element_type=jnp.float32
    )
    sparse_part = (
        jnp.zeros((tok_rows, KVH * HD // BLK, BLK), jnp.float32)
        .at[:, col_index]
        .add(block_term)
        .reshape(tok_rows, KVH * HD)
    )
    back_term = jnp.einsum("tbj,bkj->tbk", chosen, delta_values, preferred_element_type=jnp.float32)
    spread_back = (
        jnp.zeros((tok_rows, D // BLK, BLK), jnp.float32)
        .at[:, row_index]
        .add(back_term)
        .reshape(tok_rows, D)
    )
    by_shard, grad_term, sparse_part, spread_back = lax.optimization_barrier(
        (by_shard, grad_term, sparse_part, spread_back)
    )
    full_weight = gather_rest(by_shard)
    delta_grad = reduce_delta(grad_term)
    values, input_grad = dense_tail(tokens, full_weight, value_grad, spread_back, sparse_part)
    value_heads = values.reshape(tok_rows, KVH, HD)
    attention = (
        jnp.einsum("gstu,ugd->tgsd", attn_probs, value_heads, preferred_element_type=jnp.float32)
        .reshape(tok_rows, QH * HD)
        .astype(jnp.bfloat16)
    )
    return (attention, input_grad, delta_grad)


def solution(mesh):
    n_shard = mesh.shape["shard"]
    n_rep = mesh.shape["replica"]
    fine = Mesh(
        mesh.devices.reshape(2, 4, n_rep // 8, 4, n_shard // 4), ALL
    )
    tok = P(ALL, None)
    return jax.shard_map(
        local,
        mesh=fine,
        in_specs=(tok, tok, tok, tok, P(SHARD, None), P(), P(), tok),
        out_specs=(tok, tok, P(SHARD, None, None)),
        check_vma=False,
    )
```

```python
import math

import jax
import jax.numpy as jnp
from jax import lax
from jax.experimental import pallas as pl
from jax.experimental.pallas import tpu as pltpu
from jax.sharding import Mesh
from jax.sharding import PartitionSpec as P

D = 8192
QH = 64
KVH = 8
HD = 128
BLK = 64

REPLICA = ("zl", "x", "c")
SHARD = ("zh", "y")
ALL = REPLICA + SHARD
PIECE = ("x", "c")


def block_tables(block_list):
    row_hot = (block_list[:, 0:1] == jnp.arange(D // BLK, dtype=jnp.int32)[None, :]).astype(
        jnp.bfloat16
    )
    col_hot = (block_list[:, 1:2] == jnp.arange(KVH * HD // BLK, dtype=jnp.int32)[None, :]).astype(
        jnp.bfloat16
    )
    return (row_hot, col_hot)


def gather_pieces(base_weight):
    rows = base_weight.shape[0]
    pieces = lax.axis_size("x") * lax.axis_size("c")
    width = rows // pieces
    me = lax.axis_index("x") * lax.axis_size("c") + lax.axis_index("c")
    piece = lax.dynamic_slice_in_dim(base_weight, me * width, width, 0)
    return lax.all_gather(piece, SHARD, axis=0, tiled=False)


def gather_rest(by_shard):
    whole = lax.all_gather(by_shard, PIECE, axis=1, tiled=True)
    return whole.reshape(-1, whole.shape[-1])


def tail_kernel(tok_ref, w_ref, vg_ref, sb_ref, sp_ref, pr_ref, att_ref, ig_ref, acc_ref):
    k = pl.program_id(0)

    @pl.when(k == 0)
    def _():
        acc_ref[...] = sp_ref[...]

    w = w_ref[...]
    acc_ref[...] += jnp.dot(tok_ref[...], w, preferred_element_type=jnp.float32)
    back = lax.dot_general(
        vg_ref[...], w, (((1,), (1,)), ((), ())), preferred_element_type=jnp.float32
    )
    ig_ref[...] = (back + sb_ref[...]).astype(ig_ref.dtype)

    @pl.when(k == pl.num_programs(0) - 1)
    def _():
        values = acc_ref[...].astype(jnp.bfloat16)
        kv_heads, groups = pr_ref.shape[0], pr_ref.shape[1]
        for g in range(kv_heads):
            head = values[:, g * HD : (g + 1) * HD]
            for q in range(groups):
                col = (g * groups + q) * HD
                att_ref[:, col : col + HD] = jnp.dot(
                    pr_ref[g, q], head, preferred_element_type=jnp.float32
                ).astype(att_ref.dtype)


def dense_tail(tokens, full_weight, value_grad, spread_back, sparse_part, attn_probs):
    rows, depth = tokens.shape
    width = full_weight.shape[1]
    tile = 2048
    steps = depth // tile
    return pl.pallas_call(
        tail_kernel,
        grid=(steps,),
        in_specs=[
            pl.BlockSpec((rows, tile), lambda k: (0, k)),
            pl.BlockSpec((tile, width), lambda k: (k, 0)),
            pl.BlockSpec((rows, width), lambda k: (0, 0)),
            pl.BlockSpec((rows, tile), lambda k: (0, k)),
            pl.BlockSpec((rows, width), lambda k: (0, 0)),
            pl.BlockSpec(attn_probs.shape, lambda k: (0, 0, 0, 0)),
        ],
        out_specs=[
            pl.BlockSpec((rows, QH * HD), lambda k: (0, 0)),
            pl.BlockSpec((rows, tile), lambda k: (0, k)),
        ],
        out_shape=[
            jax.ShapeDtypeStruct((rows, QH * HD), jnp.bfloat16),
            jax.ShapeDtypeStruct((rows, depth), jnp.bfloat16),
        ],
        scratch_shapes=[pltpu.VMEM((rows, width), jnp.float32)],
        compiler_params=pltpu.CompilerParams(dimension_semantics=("arbitrary",)),
        cost_estimate=pl.CostEstimate(
            flops=4 * rows * depth * width,
            bytes_accessed=2 * depth * width + 8 * rows * depth + 10 * rows * width,
            transcendentals=0,
        ),
    )(tokens, full_weight, value_grad, spread_back, sparse_part, attn_probs)


def reduce_delta(grad_term):
    n_shard = lax.axis_size(SHARD)
    n_rep = lax.axis_size(REPLICA)
    nb = grad_term.shape[0]
    flat = grad_term.reshape(n_shard, -1)
    mine = lax.all_to_all(flat, SHARD, 0, 0, tiled=False).sum(0)
    mine = mine.reshape(n_rep, -1)
    part = lax.all_to_all(mine, REPLICA, 0, 0, tiled=False).sum(0)
    spread = jnp.broadcast_to(part[None], (n_rep,) + part.shape)
    whole = lax.all_to_all(spread, REPLICA, 0, 0, tiled=False)
    return whole.reshape(nb // n_shard, BLK, BLK)


def local(
    tokens,
    query_vectors,
    key_vectors,
    segment_ids,
    base_weight,
    delta_values,
    block_list,
    out_cotangent,
):
    tok_rows = tokens.shape[0]
    groups = QH // KVH
    row_index = block_list[:, 0]
    col_index = block_list[:, 1]
    by_shard = gather_pieces(base_weight)
    row_hot, col_hot = block_tables(block_list)
    picked = jnp.einsum(
        "trk,br->tbk",
        tokens.reshape(tok_rows, D // BLK, BLK),
        row_hot,
        preferred_element_type=jnp.float32,
    ).astype(jnp.bfloat16)
    query_heads = query_vectors.reshape(tok_rows, KVH, groups, HD)
    key_heads = key_vectors.reshape(tok_rows, KVH, HD)
    scores = jnp.einsum(
        "tgsd,ugd->gstu", query_heads, key_heads, preferred_element_type=jnp.float32
    ) * (1.0 / math.sqrt(HD))
    seg_row = segment_ids[0]
    position = jnp.arange(tok_rows, dtype=jnp.int32)
    allowed = (position[None, :] <= position[:, None]) & (seg_row[:, None] == seg_row[None, :])
    scores = jnp.where(allowed, scores, -1e30)
    row_max = jnp.max(scores, axis=-1, keepdims=True)
    exp_scores = jnp.exp(scores - row_max)
    attn_probs = (exp_scores / jnp.sum(exp_scores, axis=-1, keepdims=True)).astype(jnp.bfloat16)
    cotangent_heads = out_cotangent.reshape(tok_rows, KVH, groups, HD)
    value_grad = (
        jnp.einsum(
            "gstu,tgsd->ugd", attn_probs, cotangent_heads, preferred_element_type=jnp.float32
        )
        .reshape(tok_rows, KVH * HD)
        .astype(jnp.bfloat16)
    )
    chosen = jnp.einsum(
        "tcj,bc->tbj",
        value_grad.reshape(tok_rows, KVH * HD // BLK, BLK),
        col_hot,
        preferred_element_type=jnp.float32,
    ).astype(jnp.bfloat16)
    grad_scale = 1.0 / math.sqrt(tok_rows * lax.axis_size(ALL))
    grad_term = (
        jnp.einsum("tbk,tbj->bkj", picked, chosen, preferred_element_type=jnp.float32) * grad_scale
    )
    block_term = jnp.einsum(
        "tbk,bkj->tbj", picked, delta_values, preferred_element_type=jnp.float32
    )
    sparse_part = (
        jnp.zeros((tok_rows, KVH * HD // BLK, BLK), jnp.float32)
        .at[:, col_index]
        .add(block_term)
        .reshape(tok_rows, KVH * HD)
    )
    back_term = jnp.einsum("tbj,bkj->tbk", chosen, delta_values, preferred_element_type=jnp.float32)
    spread_back = (
        jnp.zeros((tok_rows, D // BLK, BLK), jnp.float32)
        .at[:, row_index]
        .add(back_term)
        .reshape(tok_rows, D)
    )
    by_shard, grad_term, sparse_part, spread_back = lax.optimization_barrier(
        (by_shard, grad_term, sparse_part, spread_back)
    )
    full_weight = gather_rest(by_shard)
    delta_grad = reduce_delta(grad_term)
    attention, input_grad = dense_tail(
        tokens, full_weight, value_grad, spread_back, sparse_part, attn_probs
    )
    return (attention, input_grad, delta_grad)


def solution(mesh):
    n_shard = mesh.shape["shard"]
    n_rep = mesh.shape["replica"]
    fine = Mesh(
        mesh.devices.reshape(2, 4, n_rep // 8, 4, n_shard // 4), ALL
    )
    tok = P(ALL, None)
    return jax.shard_map(
        local,
        mesh=fine,
        in_specs=(tok, tok, tok, tok, P(SHARD, None), P(), P(), tok),
        out_specs=(tok, tok, P(SHARD, None, None)),
        check_vma=False,
    )
```
